512 devices in a mesh: gx: 32 (over x, y), gy: 16 (over z, core).
Axes of the slice: x: 4, y: 8, z: 8, core: 2. Of those that a mesh axis runs over, the one named last changes fastest.
Arguments:
- right_side: bfloat16 [32, 16, 896, 128], P('gx', 'gy')
- schur_offdiag: bfloat16 [32, 16, 896, 896], P('gx', 'gy'), may hold values from -0.125 to 0.125
- schur_diag: float32 [32, 16, 896], P('gx', 'gy'), may hold values from 1.5 to 3
- trace_offdiag: bfloat16 [32, 16, 896, 896], P('gx', 'gy'), may hold values from -0.0390625 to 0.0390625
- trace_diag: float32 [32, 16, 896], P('gx', 'gy'), may hold values from 0.3 to 0.7
- couplings: bfloat16 [32, 16, 4, 128, 128], P('gx', 'gy'), may hold values from -0.375 to 0.375
- margin_rows: int32 [32, 16, 4, 128], P('gx', 'gy'), may hold values from 0 to 895, as said below
- deflation: bfloat16 [32, 16, 8, 896], P('gx', 'gy'), may hold values from -0.59765625 to 0.59765625
- coarse_inverse: float32 [4096, 4096], P(('gx', 'gy'))
- coarse_map: int32 [4096], replicated, may hold values from 0 to 4095, each once
Outputs:
- solution: float32 [32, 16, 896, 128], P('gx', 'gy')
- residual: float32 [32, 16, 896, 128], P('gx', 'gy')
The draws below stay inside these ranges and needn't reach their ends.
Inputs may be any that keep to these rules, and one draw needn't show every extreme that they name: `margin_rows`: the 512 rows of one subdomain's four lists are all distinct. `coarse_map`: every coarse number appears once.
All inputs are finite; a program needn't handle non-finite values.
Results may differ from the reference program's by a relative error of at most 0.022.
Values may be sent and summed in bfloat16 or wider, within the bound.
No kernel may reach another device: no remote copies, remote signals or barrier semaphores. Data moves between devices by JAX's collectives and lax.ppermute only.
A program may use at most 64 MiB of HBM per device.

```python
import math
import jax
import jax.numpy as jnp
from jax import lax

ROWS = 896
OV = 128
K = 8
SRC = 128
ITERS = 3
SUBX = 32
SUBY = 16
NC = 4096


def draw_right_side(key, part):
    key_vals = jax.random.fold_in(key, 11)
    key_rows = jax.random.fold_in(key, 12)
    key_cols = jax.random.fold_in(key, 13)
    row_scale = jnp.exp(jax.random.uniform(key_rows, (SUBX, SUBY, ROWS, 1), jnp.float32, jnp.log(0.3), jnp.log(3.0)))
    col_scale = jnp.exp(jax.random.uniform(key_cols, (1, 1, 1, SRC), jnp.float32, jnp.log(0.3), jnp.log(3.0)))
    values = jax.random.truncated_normal(key_vals, -4.0, 4.0, (SUBX, SUBY, ROWS, SRC), jnp.float32)
    return (values * row_scale * col_scale).astype(jnp.bfloat16)


def draw_margin_rows(key, part):
    keys = jax.random.split(jax.random.fold_in(key, 21), SUBX * SUBY)
    lists = jax.vmap(lambda single: jax.random.permutation(single, ROWS)[:4 * OV])(keys)
    return lists.reshape(SUBX, SUBY, 4, OV).astype(jnp.int32)


def draw_coarse_inverse(key, part):
    key_vals = jax.random.fold_in(key, 31)
    noise = jax.random.normal(key_vals, (NC, NC), jnp.float32)
    return jnp.eye(NC, dtype=jnp.float32) + noise * (1.0 / NC ** 0.5)


def block_scale(stream_key, dims, cuts, least, high):
    factor_of, own = 1.0, jax.random.fold_in(stream_key, 6)
    for axis_at, shards_of in cuts:
        draws = jnp.exp(jax.random.uniform(jax.random.fold_in(own, axis_at), (shards_of,), jnp.float32, least / len(cuts), high / len(cuts)))
        factor_of = factor_of * jnp.repeat(draws, dims[axis_at] // shards_of).reshape([-1 if axis == axis_at else 1 for axis in range(len(dims))])
    return factor_of


def normal_values(key, dims, spread, reach, cuts=(), kind=jnp.bfloat16):
    gain = block_scale(key, dims, cuts, -0.22, 0.18) if cuts else 1.0
    entries = jax.random.normal(key, dims, jnp.float32) * spread * gain
    return jnp.minimum(jnp.maximum(entries, -reach), reach).astype(kind)


def setup_inputs(seed: int = 0) -> dict:
    arg_keys = jax.random.split(jax.random.key(seed), 11)
    right_side = draw_right_side(jax.random.fold_in(arg_keys[10], 71), 0)
    schur_offdiag = normal_values(arg_keys[1], (SUBX, SUBY, ROWS, ROWS), (3 * ROWS) ** -0.5, 0.125, ((0, 32), (1, 16)))
    schur_diag = jnp.clip(jnp.exp(math.log(3.0) - 0.6931472 * jax.random.uniform(arg_keys[2], (SUBX, SUBY, ROWS), jnp.float32) ** block_scale(arg_keys[2], (SUBX, SUBY, ROWS), ((0, 32), (1, 16)), -0.2, 0.2)), 1.5, 3.0)
    trace_offdiag = normal_values(arg_keys[3], (SUBX, SUBY, ROWS, ROWS), (30 * ROWS) ** -0.5, 0.0390625, ((0, 32), (1, 16)))
    trace_diag = jnp.clip(jnp.exp(math.log(0.7) - 0.8472978 * jax.random.uniform(arg_keys[4], (SUBX, SUBY, ROWS), jnp.float32) ** block_scale(arg_keys[4], (SUBX, SUBY, ROWS), ((0, 32), (1, 16)), -0.2, 0.2)), 0.3, 0.7)
    couplings = normal_values(arg_keys[5], (SUBX, SUBY, 4, OV, OV), (2 * OV) ** -0.5, 0.375, ((0, 32), (1, 16)))
    margin_rows = draw_margin_rows(jax.random.fold_in(arg_keys[10], 71), 0)
    deflation = normal_values(arg_keys[7], (SUBX, SUBY, K, ROWS), 0.1, 0.59765625, ((0, 32), (1, 16)))
    coarse_inverse = draw_coarse_inverse(jax.random.fold_in(arg_keys[10], 71), 0)
    coarse_map = jax.random.permutation(arg_keys[9], NC).astype(jnp.int32)
    return dict(right_side=right_side, schur_offdiag=schur_offdiag, schur_diag=schur_diag, trace_offdiag=trace_offdiag, trace_diag=trace_diag, couplings=couplings, margin_rows=margin_rows, deflation=deflation, coarse_inverse=coarse_inverse, coarse_map=coarse_map)


def shift_grid(arr, axis, offset):
    count = arr.shape[axis]
    zeros = jnp.zeros_like(lax.slice_in_dim(arr, 0, 1, axis=axis))
    if offset == 1:
        return jnp.concatenate([zeros, lax.slice_in_dim(arr, 0, count - 1, axis=axis)], axis=axis)
    return jnp.concatenate([lax.slice_in_dim(arr, 1, count, axis=axis), zeros], axis=axis)


def local_products(mats, fields):
    shape = fields.shape
    flat_mats = mats.reshape((-1,) + mats.shape[2:])
    flat_fields = fields.reshape((-1,) + shape[2:])
    out = lax.map(lambda pair: jnp.dot(pair[0], pair[1], preferred_element_type=jnp.float32), (flat_mats, flat_fields))
    return out.reshape(shape)


def pick_rows(field, rows):
    return field[rows]


def add_rows(result, rows, values):
    return result.at[rows.reshape(-1)].add(-values.reshape(-1, values.shape[-1]))


def reference(right_side, schur_offdiag, schur_diag, trace_offdiag, trace_diag, couplings, margin_rows, deflation, coarse_inverse, coarse_map):
    blocks_wide = couplings.astype(jnp.float32)
    vectors = deflation.astype(jnp.float32)
    coarse_cols = jnp.take(coarse_inverse, coarse_map, axis=1)

    def apply_schur(field):
        rounded = lax.optimization_barrier(field.astype(jnp.bfloat16))
        result = schur_diag[..., None] * rounded.astype(jnp.float32) + local_products(schur_offdiag, rounded)
        sent_rows = jax.vmap(jax.vmap(pick_rows))(rounded, margin_rows)
        received = jnp.stack([shift_grid(sent_rows[:, :, 1], 0, 1), shift_grid(sent_rows[:, :, 0], 0, -1),
                              shift_grid(sent_rows[:, :, 3], 1, 1), shift_grid(sent_rows[:, :, 2], 1, -1)], axis=2)
        coupled = jnp.einsum("xydab,xydbs->xydas", blocks_wide, received.astype(jnp.float32))
        return jax.vmap(jax.vmap(add_rows))(result, margin_rows, coupled)

    def apply_prec(field):
        rounded = lax.optimization_barrier(field.astype(jnp.bfloat16))
        result = trace_diag[..., None] * rounded.astype(jnp.float32) + local_products(trace_offdiag, rounded)
        coarse = jnp.einsum("xykr,xyrs->xyks", vectors, rounded.astype(jnp.float32))
        stacked = coarse.reshape(-1, coarse.shape[-1])
        solved = jnp.dot(coarse_cols, stacked, precision=lax.Precision.HIGHEST).reshape(coarse.shape)
        return result + jnp.einsum("xykr,xyks->xyrs", vectors, solved, precision=lax.Precision.HIGHEST)

    rhs_wide = right_side.astype(jnp.float32)
    solution = jnp.zeros(right_side.shape, jnp.float32)
    direction = apply_prec(rhs_wide)
    for iteration in range(ITERS):
        image = apply_schur(direction)
        mapped = apply_prec(image)
        numer = jnp.sum(mapped * direction, axis=(0, 1, 2))
        denom = jnp.sum(mapped * mapped, axis=(0, 1, 2))
        alpha = numer / denom
        solution = solution + alpha * direction
        direction = direction - alpha * mapped
    residual = rhs_wide - apply_schur(solution)
    return solution, residual
```

```python
import jax
import jax.numpy as jnp
from jax import lax
from jax.sharding import PartitionSpec as P

ITERS = 3


def from_behind(value, axis, steps):
    count = lax.axis_size(axis)
    leading, last = (max(0, -steps), min(count, count - steps))
    return lax.ppermute(value, axis, [(source, source + steps) for source in range(leading, last)])


def total_over_mesh(value):
    for axis in ("gy", "gx"):
        count = lax.axis_size(axis)
        step = 1
        while step < count:
            value = value + lax.ppermute(value, axis, [(i, i ^ step) for i in range(count)])
            step *= 2
    return value


def pass_columns(rows, offset):
    return from_behind(rows, "gx", offset)


def pass_lines(rows, offset):
    return from_behind(rows, "gy", offset)


def shards(
    right_side,
    schur_offdiag,
    schur_diag,
    trace_offdiag,
    trace_diag,
    couplings,
    margin_rows,
    deflation,
    coarse_inverse,
    coarse_map,
):
    rhs_wide = right_side[0, 0].astype(jnp.float32)
    schur_mat = schur_offdiag[0, 0]
    schur_scale = schur_diag[0, 0][:, None]
    trace_mat = trace_offdiag[0, 0]
    trace_scale = trace_diag[0, 0][:, None]
    coupling_blocks = couplings[0, 0]
    rows_lists = margin_rows[0, 0]
    flat_rows = rows_lists.reshape(-1)
    vectors = deflation[0, 0]
    vectors_wide = vectors.astype(jnp.float32).T
    coarse_cols = jnp.take(coarse_inverse, coarse_map, axis=1)

    def apply_schur(field):
        rounded = lax.optimization_barrier(field.astype(jnp.bfloat16))
        result = schur_scale * rounded.astype(jnp.float32) + jnp.dot(
            schur_mat, rounded, preferred_element_type=jnp.float32
        )
        sent_rows = rounded[rows_lists]
        received = jnp.stack(
            [
                pass_columns(sent_rows[1], 1),
                pass_columns(sent_rows[0], -1),
                pass_lines(sent_rows[3], 1),
                pass_lines(sent_rows[2], -1),
            ]
        )
        coupled = jnp.einsum(
            "dab,dbs->das", coupling_blocks, received, preferred_element_type=jnp.float32
        )
        return result.at[flat_rows].add(-coupled.reshape(-1, coupled.shape[-1]))

    def apply_prec(field):
        rounded = lax.optimization_barrier(field.astype(jnp.bfloat16))
        result = trace_scale * rounded.astype(jnp.float32) + jnp.dot(
            trace_mat, rounded, preferred_element_type=jnp.float32
        )
        coarse = jnp.dot(vectors, rounded, preferred_element_type=jnp.float32)
        stacked = lax.all_gather(
            lax.all_gather(coarse, "gx", axis=0), "gy", axis=1
        ).reshape(-1, coarse.shape[-1])
        solved = jnp.dot(coarse_cols, stacked, precision=lax.Precision.HIGHEST)
        return result + jnp.dot(vectors_wide, solved, precision=lax.Precision.HIGHEST)

    solution = jnp.zeros(rhs_wide.shape, jnp.float32)
    direction = apply_prec(rhs_wide)
    for iteration in range(ITERS):
        image = apply_schur(direction)
        mapped = apply_prec(image)
        numer, denom = total_over_mesh(
            jnp.stack([jnp.sum(mapped * direction, axis=0), jnp.sum(mapped * mapped, axis=0)])
        )
        alpha = numer / denom
        solution = solution + alpha * direction
        direction = direction - alpha * mapped
    residual = rhs_wide - apply_schur(solution)
    return (solution[None, None], residual[None, None])


def solution(mesh):
    return jax.shard_map(
        shards,
        mesh=mesh,
        in_specs=(
            P("gx", "gy", None, None),
            P("gx", "gy", None, None),
            P("gx", "gy", None),
            P("gx", "gy", None, None),
            P("gx", "gy", None),
            P("gx", "gy", None, None, None),
            P("gx", "gy", None, None),
            P("gx", "gy", None, None),
            P(("gx", "gy"), None),
            P(),
        ),
        out_specs=(P("gx", "gy", None, None), P("gx", "gy", None, None)),
        check_vma=False,
    )
```

```python
import jax
import jax.numpy as jnp
from jax import lax
from jax.sharding import PartitionSpec as P

ITERS = 3


def from_behind(value, axis, steps):
    count = lax.axis_size(axis)
    leading, last = (max(0, -steps), min(count, count - steps))
    return lax.ppermute(value, axis, [(source, source + steps) for source in range(leading, last)])


def total_over_mesh(value):
    for axis in ("gy", "gx"):
        count = lax.axis_size(axis)
        step = 1
        while step < count:
            value = value + lax.ppermute(value, axis, [(i, i ^ step) for i in range(count)])
            step *= 2
    return value


def scatter_rows(stacked, axis, rows):
    count = lax.axis_size(axis)
    index = lax.axis_index(axis)
    blocks = stacked.reshape(count, rows, stacked.shape[-1])
    half = count // 2
    while half >= 1:
        upper = (index // half) % 2 == 1
        keep = jnp.where(upper, blocks[half:], blocks[:half])
        send = jnp.where(upper, blocks[:half], blocks[half:])
        blocks = keep + lax.ppermute(send, axis, [(i, i ^ half) for i in range(count)])
        half //= 2
    return blocks[0]


def pass_columns(rows, offset):
    return from_behind(rows, "gx", offset)


def pass_lines(rows, offset):
    return from_behind(rows, "gy", offset)


def shards(
    right_side,
    schur_offdiag,
    schur_diag,
    trace_offdiag,
    trace_diag,
    couplings,
    margin_rows,
    deflation,
    coarse_inverse,
    coarse_map,
):
    rhs_wide = right_side[0, 0].astype(jnp.float32)
    schur_mat = schur_offdiag[0, 0]
    schur_scale = schur_diag[0, 0][:, None]
    trace_mat = trace_offdiag[0, 0]
    trace_scale = trace_diag[0, 0][:, None]
    coupling_blocks = couplings[0, 0]
    rows_lists = margin_rows[0, 0]
    flat_rows = rows_lists.reshape(-1)
    vectors = deflation[0, 0]
    vectors_wide = vectors.astype(jnp.float32).T
    count_x, count_y = lax.axis_size("gx"), lax.axis_size("gy")
    depth = vectors.shape[0]
    coarse_cols = jnp.take(coarse_inverse, coarse_map, axis=1)
    coarse_block = lax.all_to_all(
        coarse_cols.reshape(depth, count_x, count_y * depth), "gx", 1, 0, tiled=True
    ).reshape(count_x * depth, count_y * depth)

    def apply_schur(field):
        rounded = lax.optimization_barrier(field.astype(jnp.bfloat16))
        result = schur_scale * rounded.astype(jnp.float32) + jnp.dot(
            schur_mat, rounded, preferred_element_type=jnp.float32
        )
        sent_rows = rounded[rows_lists]
        received = jnp.stack(
            [
                pass_columns(sent_rows[1], 1),
                pass_columns(sent_rows[0], -1),
                pass_lines(sent_rows[3], 1),
                pass_lines(sent_rows[2], -1),
            ]
        )
        coupled = jnp.einsum(
            "dab,dbs->das", coupling_blocks, received, preferred_element_type=jnp.float32
        )
        return result.at[flat_rows].add(-coupled.reshape(-1, coupled.shape[-1]))

    def apply_prec(field):
        rounded = lax.optimization_barrier(field.astype(jnp.bfloat16))
        result = trace_scale * rounded.astype(jnp.float32) + jnp.dot(
            trace_mat, rounded, preferred_element_type=jnp.float32
        )
        coarse = jnp.dot(vectors, rounded, preferred_element_type=jnp.float32)
        line = lax.all_gather(coarse, "gy", axis=0, tiled=True)
        partial = jnp.dot(coarse_block, line, precision=lax.Precision.HIGHEST)
        solved = scatter_rows(partial, "gx", depth)
        return result + jnp.dot(vectors_wide, solved, precision=lax.Precision.HIGHEST)

    solution = jnp.zeros(rhs_wide.shape, jnp.float32)
    direction = apply_prec(rhs_wide)
    for iteration in range(ITERS):
        image = apply_schur(direction)
        mapped = apply_prec(image)
        numer, denom = total_over_mesh(
            jnp.stack([jnp.sum(mapped * direction, axis=0), jnp.sum(mapped * mapped, axis=0)])
        )
        alpha = numer / denom
        solution = solution + alpha * direction
        direction = direction - alpha * mapped
    residual = rhs_wide - apply_schur(solution)
    return (solution[None, None], residual[None, None])


def solution(mesh):
    return jax.shard_map(
        shards,
        mesh=mesh,
        in_specs=(
            P("gx", "gy", None, None),
            P("gx", "gy", None, None),
            P("gx", "gy", None),
            P("gx", "gy", None, None),
            P("gx", "gy", None),
            P("gx", "gy", None, None, None),
            P("gx", "gy", None, None),
            P("gx", "gy", None, None),
            P(("gx", "gy"), None),
            P(),
        ),
        out_specs=(P("gx", "gy", None, None), P("gx", "gy", None, None)),
        check_vma=False,
    )
```

```python
import jax
import jax.numpy as jnp
from jax import lax
from jax.sharding import PartitionSpec as P

ITERS = 3


def from_behind(value, axis, steps):
    count = lax.axis_size(axis)
    leading, last = (max(0, -steps), min(count, count - steps))
    return lax.ppermute(value, axis, [(source, source + steps) for source in range(leading, last)])


def total_over_mesh(value, tie):
    value = jnp.sum(lax.all_gather(value, "gy", axis=0), axis=0)
    count = lax.axis_size("gx")
    step = 1
    while step < count:
        if step == count // 2:
            value = value + 0.0 * tie
        value = value + lax.ppermute(value, "gx", [(i, i ^ step) for i in range(count)])
        step *= 2
    return value


def scatter_rows(stacked, axis, rows):
    count = lax.axis_size(axis)
    index = lax.axis_index(axis)
    blocks = stacked.reshape(count, rows, stacked.shape[-1])
    half = count // 2
    while half >= 1:
        upper = (index // half) % 2 == 1
        keep = jnp.where(upper, blocks[half:], blocks[:half])
        send = jnp.where(upper, blocks[:half], blocks[half:])
        blocks = keep + lax.ppermute(send, axis, [(i, i ^ half) for i in range(count)])
        half //= 2
    return blocks[0]


def pass_columns(rows, offset):
    return from_behind(rows, "gx", offset)


def pass_lines(rows, offset):
    return from_behind(rows, "gy", offset)


def shards(
    right_side,
    schur_offdiag,
    schur_diag,
    trace_offdiag,
    trace_diag,
    couplings,
    margin_rows,
    deflation,
    coarse_inverse,
    coarse_map,
):
    rhs_wide = right_side[0, 0].astype(jnp.float32)
    schur_mat = schur_offdiag[0, 0]
    schur_scale = schur_diag[0, 0][:, None]
    trace_mat = trace_offdiag[0, 0]
    trace_scale = trace_diag[0, 0][:, None]
    coupling_blocks = couplings[0, 0]
    rows_lists = margin_rows[0, 0]
    flat_rows = rows_lists.reshape(-1)
    vectors = deflation[0, 0]
    vectors_wide = vectors.astype(jnp.float32).T
    count_x, count_y = lax.axis_size("gx"), lax.axis_size("gy")
    depth = vectors.shape[0]
    coarse_cols = jnp.take(coarse_inverse, coarse_map, axis=1)
    coarse_block = lax.all_to_all(
        coarse_cols.reshape(depth, count_x, count_y * depth), "gx", 1, 0, tiled=True
    ).reshape(count_x * depth, count_y * depth)

    def exchange(sent_rows):
        return jnp.stack(
            [
                pass_columns(sent_rows[1], 1),
                pass_columns(sent_rows[0], -1),
                pass_lines(sent_rows[3], 1),
                pass_lines(sent_rows[2], -1),
            ]
        )

    def finish_schur(rounded, received):
        result = schur_scale * rounded.astype(jnp.float32) + jnp.dot(
            schur_mat, rounded, preferred_element_type=jnp.float32
        )
        coupled = jnp.einsum(
            "dab,dbs->das", coupling_blocks, received, preferred_element_type=jnp.float32
        )
        return result.at[flat_rows].add(-coupled.reshape(-1, coupled.shape[-1]))

    def apply_schur(field):
        rounded = lax.optimization_barrier(field.astype(jnp.bfloat16))
        return finish_schur(rounded, exchange(rounded[rows_lists]))

    def send_early(base, step):
        return exchange(jnp.stack([base[rows_lists], step[rows_lists]], axis=1))

    def apply_schur_late(field, pair, coef):
        rounded = lax.optimization_barrier(field.astype(jnp.bfloat16))
        received = (pair[:, 0] + coef * pair[:, 1]).astype(jnp.bfloat16)
        return finish_schur(rounded, received)

    def apply_prec(field):
        rounded = lax.optimization_barrier(field.astype(jnp.bfloat16))
        result = trace_scale * rounded.astype(jnp.float32) + jnp.dot(
            trace_mat, rounded, preferred_element_type=jnp.float32
        )
        coarse = jnp.dot(vectors, rounded, preferred_element_type=jnp.float32)
        line = lax.all_gather(coarse, "gy", axis=0, tiled=True)
        partial = jnp.dot(coarse_block, line, precision=lax.Precision.HIGHEST)
        solved = scatter_rows(partial, "gx", depth)
        return result + jnp.dot(vectors_wide, solved, precision=lax.Precision.HIGHEST)

    solution = jnp.zeros(rhs_wide.shape, jnp.float32)
    direction = apply_prec(rhs_wide)
    image = apply_schur(direction)
    for iteration in range(ITERS):
        mapped = apply_prec(image)
        if iteration + 1 < ITERS:
            pair = send_early(direction, mapped)
        else:
            pair = send_early(solution, direction)
        numer, denom = total_over_mesh(
            jnp.stack([jnp.sum(mapped * direction, axis=0), jnp.sum(mapped * mapped, axis=0)]),
            jnp.sum(pair[:, 0, 0, 0]),
        )
        alpha = numer / denom
        solution = solution + alpha * direction
        direction = direction + (-alpha) * mapped
        if iteration + 1 < ITERS:
            image = apply_schur_late(direction, pair, -alpha)
    residual = rhs_wide - apply_schur_late(solution, pair, alpha)
    return (solution[None, None], residual[None, None])


def solution(mesh):
    return jax.shard_map(
        shards,
        mesh=mesh,
        in_specs=(
            P("gx", "gy", None, None),
            P("gx", "gy", None, None),
            P("gx", "gy", None),
            P("gx", "gy", None, None),
            P("gx", "gy", None),
            P("gx", "gy", None, None, None),
            P("gx", "gy", None, None),
            P("gx", "gy", None, None),
            P(("gx", "gy"), None),
            P(),
        ),
        out_specs=(P("gx", "gy", None, None), P("gx", "gy", None, None)),
        check_vma=False,
    )
```

```python
import jax
import jax.numpy as jnp
from jax import lax
from jax.sharding import PartitionSpec as P

ITERS = 3


def from_behind(value, axis, steps):
    count = lax.axis_size(axis)
    leading, last = (max(0, -steps), min(count, count - steps))
    return lax.ppermute(value, axis, [(source, source + steps) for source in range(leading, last)])


def digit_sizes(count):
    sizes, size = [], count
    while size > 1:
        radix = 4 if size % 4 == 0 else 2
        size //= radix
        sizes.append((radix, size))
    return sizes


def total_over_mesh(value, tie):
    value = jnp.sum(lax.all_gather(value, "gy", axis=0), axis=0)
    count = lax.axis_size("gx")
    index = lax.axis_index("gx")
    sizes = digit_sizes(count)
    for position, (radix, size) in enumerate(sizes):
        if position == len(sizes) - 1:
            value = value + 0.0 * tie
        parts = [value] + [
            lax.ppermute(value, "gx", [(i, i ^ (j * size)) for i in range(count)]) for j in range(1, radix)
        ]
        own = (index // size) % radix
        ordered = jnp.stack(parts)[jnp.arange(radix) ^ own]
        while ordered.shape[0] > 1:
            ordered = ordered[0::2] + ordered[1::2]
        value = ordered[0]
    return value


def scatter_rows(stacked, axis, rows):
    count = lax.axis_size(axis)
    index = lax.axis_index(axis)
    blocks = stacked.reshape(count, rows, stacked.shape[-1])
    for radix, size in digit_sizes(count):
        own = (index // size) % radix
        quarters = blocks.reshape((radix, size) + blocks.shape[1:])
        total = jnp.take(quarters, own, axis=0)
        for j in range(1, radix):
            send = jnp.take(quarters, own ^ j, axis=0)
            total = total + lax.ppermute(send, axis, [(i, i ^ (j * size)) for i in range(count)])
        blocks = total
    return blocks[0]


def pass_columns(rows, offset):
    return from_behind(rows, "gx", offset)


def pass_lines(rows, offset):
    return from_behind(rows, "gy", offset)


def shards(
    right_side,
    schur_offdiag,
    schur_diag,
    trace_offdiag,
    trace_diag,
    couplings,
    margin_rows,
    deflation,
    coarse_inverse,
    coarse_map,
):
    rhs_wide = right_side[0, 0].astype(jnp.float32)
    schur_mat = schur_offdiag[0, 0]
    schur_scale = schur_diag[0, 0][:, None]
    trace_mat = trace_offdiag[0, 0]
    trace_scale = trace_diag[0, 0][:, None]
    coupling_blocks = couplings[0, 0]
    rows_lists = margin_rows[0, 0]
    flat_rows = rows_lists.reshape(-1)
    vectors = deflation[0, 0]
    vectors_wide = vectors.astype(jnp.float32).T
    count_x, count_y = lax.axis_size("gx"), lax.axis_size("gy")
    depth = vectors.shape[0]
    coarse_cols = jnp.take(coarse_inverse, coarse_map, axis=1)
    coarse_block = lax.all_to_all(
        coarse_cols.reshape(depth, count_x, count_y * depth), "gx", 1, 0, tiled=True
    ).reshape(count_x * depth, count_y * depth)

    def exchange(sent_rows):
        return jnp.stack(
            [
                pass_columns(sent_rows[1], 1),
                pass_columns(sent_rows[0], -1),
                pass_lines(sent_rows[3], 1),
                pass_lines(sent_rows[2], -1),
            ]
        )

    def finish_schur(rounded, received):
        result = schur_scale * rounded.astype(jnp.float32) + jnp.dot(
            schur_mat, rounded, preferred_element_type=jnp.float32
        )
        coupled = jnp.einsum(
            "dab,dbs->das", coupling_blocks, received, preferred_element_type=jnp.float32
        )
        return result.at[flat_rows].add(-coupled.reshape(-1, coupled.shape[-1]))

    def apply_schur(field):
        rounded = lax.optimization_barrier(field.astype(jnp.bfloat16))
        return finish_schur(rounded, exchange(rounded[rows_lists]))

    def send_early(base, step):
        return exchange(jnp.stack([base[rows_lists], step[rows_lists]], axis=1))

    def apply_schur_late(field, pair, coef):
        rounded = lax.optimization_barrier(field.astype(jnp.bfloat16))
        received = (pair[:, 0] + coef * pair[:, 1]).astype(jnp.bfloat16)
        return finish_schur(rounded, received)

    def apply_prec(field):
        rounded = lax.optimization_barrier(field.astype(jnp.bfloat16))
        result = trace_scale * rounded.astype(jnp.float32) + jnp.dot(
            trace_mat, rounded, preferred_element_type=jnp.float32
        )
        coarse = jnp.dot(vectors, rounded, preferred_element_type=jnp.float32)
        line = lax.all_gather(coarse, "gy", axis=0, tiled=True)
        partial = jnp.dot(coarse_block, line, precision=lax.Precision.HIGHEST)
        solved = scatter_rows(partial, "gx", depth)
        return result + jnp.dot(vectors_wide, solved, precision=lax.Precision.HIGHEST)

    solution = jnp.zeros(rhs_wide.shape, jnp.float32)
    direction = apply_prec(rhs_wide)
    image = apply_schur(direction)
    for iteration in range(ITERS):
        mapped = apply_prec(image)
        if iteration + 1 < ITERS:
            pair = send_early(direction, mapped)
        else:
            pair = send_early(solution, direction)
        numer, denom = total_over_mesh(
            jnp.stack([jnp.sum(mapped * direction, axis=0), jnp.sum(mapped * mapped, axis=0)]),
            jnp.sum(pair[:, 0, 0, 0]),
        )
        alpha = numer / denom
        solution = solution + alpha * direction
        direction = direction + (-alpha) * mapped
        if iteration + 1 < ITERS:
            image = apply_schur_late(direction, pair, -alpha)
    residual = rhs_wide - apply_schur_late(solution, pair, alpha)
    return (solution[None, None], residual[None, None])


def solution(mesh):
    return jax.shard_map(
        shards,
        mesh=mesh,
        in_specs=(
            P("gx", "gy", None, None),
            P("gx", "gy", None, None),
            P("gx", "gy", None),
            P("gx", "gy", None, None),
            P("gx", "gy", None),
            P("gx", "gy", None, None, None),
            P("gx", "gy", None, None),
            P("gx", "gy", None, None),
            P(("gx", "gy"), None),
            P(),
        ),
        out_specs=(P("gx", "gy", None, None), P("gx", "gy", None, None)),
        check_vma=False,
    )
```

```python
import jax
import jax.numpy as jnp
from jax import lax
from jax.sharding import PartitionSpec as P

ITERS = 3


def from_behind(value, axis, steps):
    count = lax.axis_size(axis)
    leading, last = (max(0, -steps), min(count, count - steps))
    return lax.ppermute(value, axis, [(source, source + steps) for source in range(leading, last)])


def total_over_mesh(value, tie):
    value = jnp.sum(lax.all_gather(value, "gy", axis=0), axis=0)
    count = lax.axis_size("gx")
    step = 1
    while step < count:
        if step == count // 2:
            value = value + 0.0 * tie
        value = value + lax.ppermute(value, "gx", [(i, i ^ step) for i in range(count)])
        step *= 2
    return value


def pass_columns(rows, offset):
    return from_behind(rows, "gx", offset)


def pass_lines(rows, offset):
    return from_behind(rows, "gy", offset)


def shards(
    right_side,
    schur_offdiag,
    schur_diag,
    trace_offdiag,
    trace_diag,
    couplings,
    margin_rows,
    deflation,
    coarse_inverse,
    coarse_map,
):
    rhs_wide = right_side[0, 0].astype(jnp.float32)
    schur_mat = schur_offdiag[0, 0]
    schur_scale = schur_diag[0, 0][:, None]
    trace_mat = trace_offdiag[0, 0]
    trace_scale = trace_diag[0, 0][:, None]
    coupling_blocks = couplings[0, 0]
    rows_lists = margin_rows[0, 0]
    flat_rows = rows_lists.reshape(-1)
    vectors = deflation[0, 0]
    vectors_wide = vectors.astype(jnp.float32).T
    count_x, count_y = lax.axis_size("gx"), lax.axis_size("gy")
    depth = vectors.shape[0]
    coarse_cols = jnp.take(coarse_inverse, coarse_map, axis=1)
    coarse_block = lax.all_to_all(
        coarse_cols.reshape(depth, count_x, count_y * depth), "gx", 1, 0, tiled=True
    ).reshape(count_x * depth, count_y * depth)

    def exchange(sent_rows):
        return jnp.stack(
            [
                pass_columns(sent_rows[1], 1),
                pass_columns(sent_rows[0], -1),
                pass_lines(sent_rows[3], 1),
                pass_lines(sent_rows[2], -1),
            ]
        )

    def finish_schur(rounded, received):
        result = schur_scale * rounded.astype(jnp.float32) + jnp.dot(
            schur_mat, rounded, preferred_element_type=jnp.float32
        )
        coupled = jnp.einsum(
            "dab,dbs->das", coupling_blocks, received, preferred_element_type=jnp.float32
        )
        return result.at[flat_rows].add(-coupled.reshape(-1, coupled.shape[-1]))

    def apply_schur(field):
        rounded = lax.optimization_barrier(field.astype(jnp.bfloat16))
        return finish_schur(rounded, exchange(rounded[rows_lists]))

    def send_early(base, step):
        return exchange(jnp.stack([base[rows_lists], step[rows_lists]], axis=1))

    def apply_schur_late(field, pair, coef):
        rounded = lax.optimization_barrier(field.astype(jnp.bfloat16))
        received = (pair[:, 0] + coef * pair[:, 1]).astype(jnp.bfloat16)
        return finish_schur(rounded, received)

    def apply_prec(field):
        rounded = lax.optimization_barrier(field.astype(jnp.bfloat16))
        result = trace_scale * rounded.astype(jnp.float32) + jnp.dot(
            trace_mat, rounded, preferred_element_type=jnp.float32
        )
        coarse = jnp.dot(vectors, rounded, preferred_element_type=jnp.float32)
        line = lax.all_gather(coarse, "gy", axis=0, tiled=True)
        partial = jnp.dot(coarse_block, line, precision=lax.Precision.HIGHEST)
        pieces = lax.all_to_all(partial, "gx", 0, 0, tiled=True)
        solved = jnp.sum(pieces.reshape(count_x, depth, pieces.shape[-1]), axis=0)
        return result + jnp.dot(vectors_wide, solved, precision=lax.Precision.HIGHEST)

    solution = jnp.zeros(rhs_wide.shape, jnp.float32)
    direction = apply_prec(rhs_wide)
    image = apply_schur(direction)
    for iteration in range(ITERS):
        mapped = apply_prec(image)
        if iteration + 1 < ITERS:
            pair = send_early(direction, mapped)
        else:
            pair = send_early(solution, direction)
        numer, denom = total_over_mesh(
            jnp.stack([jnp.sum(mapped * direction, axis=0), jnp.sum(mapped * mapped, axis=0)]),
            jnp.sum(pair[:, 0, 0, 0]),
        )
        alpha = numer / denom
        solution = solution + alpha * direction
        direction = direction + (-alpha) * mapped
        if iteration + 1 < ITERS:
            image = apply_schur_late(direction, pair, -alpha)
    residual = rhs_wide - apply_schur_late(solution, pair, alpha)
    return (solution[None, None], residual[None, None])


def solution(mesh):
    return jax.shard_map(
        shards,
        mesh=mesh,
        in_specs=(
            P("gx", "gy", None, None),
            P("gx", "gy", None, None),
            P("gx", "gy", None),
            P("gx", "gy", None, None),
            P("gx", "gy", None),
            P("gx", "gy", None, None, None),
            P("gx", "gy", None, None),
            P("gx", "gy", None, None),
            P(("gx", "gy"), None),
            P(),
        ),
        out_specs=(P("gx", "gy", None, None), P("gx", "gy", None, None)),
        check_vma=False,
    )
```

```python
import jax
import jax.numpy as jnp
from jax import lax
from jax.sharding import PartitionSpec as P

ITERS = 3


def from_behind(value, axis, steps):
    count = lax.axis_size(axis)
    leading, last = (max(0, -steps), min(count, count - steps))
    return lax.ppermute(value, axis, [(source, source + steps) for source in range(leading, last)])


def gather_rows(value, axis):
    count = lax.axis_size(axis)
    copies = jnp.broadcast_to(value[None], (count,) + value.shape)
    return lax.all_to_all(copies.reshape((-1,) + value.shape[1:]), axis, 0, 0, tiled=True)


def total_over_mesh(value, tie):
    for axis in ("gy", "gx"):
        if axis == "gx":
            value = value + 0.0 * tie
        count = lax.axis_size(axis)
        value = jnp.sum(gather_rows(value, axis).reshape((count,) + value.shape), axis=0)
    return value


def pass_columns(rows, offset):
    return from_behind(rows, "gx", offset)


def pass_lines(rows, offset):
    return from_behind(rows, "gy", offset)


def shards(
    right_side,
    schur_offdiag,
    schur_diag,
    trace_offdiag,
    trace_diag,
    couplings,
    margin_rows,
    deflation,
    coarse_inverse,
    coarse_map,
):
    rhs_wide = right_side[0, 0].astype(jnp.float32)
    schur_mat = schur_offdiag[0, 0]
    schur_scale = schur_diag[0, 0][:, None]
    trace_mat = trace_offdiag[0, 0]
    trace_scale = trace_diag[0, 0][:, None]
    coupling_blocks = couplings[0, 0]
    rows_lists = margin_rows[0, 0]
    flat_rows = rows_lists.reshape(-1)
    vectors = deflation[0, 0]
    vectors_wide = vectors.astype(jnp.float32).T
    count_x, count_y = lax.axis_size("gx"), lax.axis_size("gy")
    depth = vectors.shape[0]
    coarse_cols = jnp.take(coarse_inverse, coarse_map, axis=1)
    coarse_block = lax.all_to_all(
        coarse_cols.reshape(depth, count_x, count_y * depth), "gx", 1, 0, tiled=True
    ).reshape(count_x * depth, count_y * depth)

    def exchange(sent_rows):
        return jnp.stack(
            [
                pass_columns(sent_rows[1], 1),
                pass_columns(sent_rows[0], -1),
                pass_lines(sent_rows[3], 1),
                pass_lines(sent_rows[2], -1),
            ]
        )

    def finish_schur(rounded, received):
        result = schur_scale * rounded.astype(jnp.float32) + jnp.dot(
            schur_mat, rounded, preferred_element_type=jnp.float32
        )
        coupled = jnp.einsum(
            "dab,dbs->das", coupling_blocks, received, preferred_element_type=jnp.float32
        )
        return result.at[flat_rows].add(-coupled.reshape(-1, coupled.shape[-1]))

    def apply_schur(field):
        rounded = lax.optimization_barrier(field.astype(jnp.bfloat16))
        return finish_schur(rounded, exchange(rounded[rows_lists]))

    def send_early(base, step):
        return exchange(jnp.stack([base[rows_lists], step[rows_lists]], axis=1))

    def apply_schur_late(field, pair, coef):
        rounded = lax.optimization_barrier(field.astype(jnp.bfloat16))
        received = (pair[:, 0] + coef * pair[:, 1]).astype(jnp.bfloat16)
        return finish_schur(rounded, received)

    def apply_prec(field):
        rounded = lax.optimization_barrier(field.astype(jnp.bfloat16))
        result = trace_scale * rounded.astype(jnp.float32) + jnp.dot(
            trace_mat, rounded, preferred_element_type=jnp.float32
        )
        coarse = jnp.dot(vectors, rounded, preferred_element_type=jnp.float32)
        line = gather_rows(coarse, "gy")
        partial = jnp.dot(coarse_block, line, precision=lax.Precision.HIGHEST)
        pieces = lax.all_to_all(partial, "gx", 0, 0, tiled=True)
        solved = jnp.sum(pieces.reshape(count_x, depth, pieces.shape[-1]), axis=0)
        return result + jnp.dot(vectors_wide, solved, precision=lax.Precision.HIGHEST)

    solution = jnp.zeros(rhs_wide.shape, jnp.float32)
    direction = apply_prec(rhs_wide)
    image = apply_schur(direction)
    for iteration in range(ITERS):
        mapped = apply_prec(image)
        if iteration + 1 < ITERS:
            pair = send_early(direction, mapped)
        else:
            pair = send_early(solution, direction)
        numer, denom = total_over_mesh(
            jnp.stack([jnp.sum(mapped * direction, axis=0), jnp.sum(mapped * mapped, axis=0)]),
            jnp.sum(pair[:, 0, 0, 0]),
        )
        alpha = numer / denom
        solution = solution + alpha * direction
        direction = direction + (-alpha) * mapped
        if iteration + 1 < ITERS:
            image = apply_schur_late(direction, pair, -alpha)
    residual = rhs_wide - apply_schur_late(solution, pair, alpha)
    return (solution[None, None], residual[None, None])


def solution(mesh):
    return jax.shard_map(
        shards,
        mesh=mesh,
        in_specs=(
            P("gx", "gy", None, None),
            P("gx", "gy", None, None),
            P("gx", "gy", None),
            P("gx", "gy", None, None),
            P("gx", "gy", None),
            P("gx", "gy", None, None, None),
            P("gx", "gy", None, None),
            P("gx", "gy", None, None),
            P(("gx", "gy"), None),
            P(),
        ),
        out_specs=(P("gx", "gy", None, None), P("gx", "gy", None, None)),
        check_vma=False,
    )
```

```python
import jax
import jax.numpy as jnp
from jax import lax
from jax.sharding import PartitionSpec as P

ITERS = 3


def from_behind(value, axis, steps):
    count = lax.axis_size(axis)
    leading, last = (max(0, -steps), min(count, count - steps))
    return lax.ppermute(value, axis, [(source, source + steps) for source in range(leading, last)])


def gather_rows(value, axis):
    count = lax.axis_size(axis)
    copies = jnp.broadcast_to(value[None], (count,) + value.shape)
    return lax.all_to_all(copies.reshape((-1,) + value.shape[1:]), axis, 0, 0, tiled=True)


def total_over_axis(value, axis):
    count = lax.axis_size(axis)
    return jnp.sum(gather_rows(value, axis).reshape((count,) + value.shape), axis=0)


def pass_columns(rows, offset):
    return from_behind(rows, "gx", offset)


def pass_lines(rows, offset):
    return from_behind(rows, "gy", offset)


def shards(
    right_side,
    schur_offdiag,
    schur_diag,
    trace_offdiag,
    trace_diag,
    couplings,
    margin_rows,
    deflation,
    coarse_inverse,
    coarse_map,
):
    rhs_wide = right_side[0, 0].astype(jnp.float32)
    schur_mat = schur_offdiag[0, 0]
    schur_scale = schur_diag[0, 0][:, None]
    trace_mat = trace_offdiag[0, 0]
    trace_scale = trace_diag[0, 0][:, None]
    coupling_blocks = couplings[0, 0]
    rows_lists = margin_rows[0, 0]
    flat_rows = rows_lists.reshape(-1)
    vectors = deflation[0, 0]
    vectors_wide = vectors.astype(jnp.float32).T
    count_x, count_y = lax.axis_size("gx"), lax.axis_size("gy")
    depth = vectors.shape[0]
    coarse_cols = jnp.take(coarse_inverse, coarse_map, axis=1)
    coarse_block = lax.all_to_all(
        coarse_cols.reshape(depth, count_x, count_y * depth), "gx", 1, 0, tiled=True
    ).reshape(count_x * depth, count_y * depth)

    def exchange(sent_rows):
        return jnp.stack(
            [
                pass_columns(sent_rows[1], 1),
                pass_columns(sent_rows[0], -1),
                pass_lines(sent_rows[3], 1),
                pass_lines(sent_rows[2], -1),
            ]
        )

    def finish_schur(rounded, received):
        result = schur_scale * rounded.astype(jnp.float32) + jnp.dot(
            schur_mat, rounded, preferred_element_type=jnp.float32
        )
        coupled = jnp.einsum(
            "dab,dbs->das", coupling_blocks, received, preferred_element_type=jnp.float32
        )
        return result.at[flat_rows].add(-coupled.reshape(-1, coupled.shape[-1]))

    def apply_schur(field):
        rounded = lax.optimization_barrier(field.astype(jnp.bfloat16))
        return finish_schur(rounded, exchange(rounded[rows_lists]))

    def send_early(base, step, after):
        rows = jnp.stack([base[rows_lists], step[rows_lists]], axis=1)
        return exchange(rows + 0.0 * after)

    def apply_schur_late(field, pair, coef):
        rounded = lax.optimization_barrier(field.astype(jnp.bfloat16))
        received = (pair[:, 0] + coef * pair[:, 1]).astype(jnp.bfloat16)
        return finish_schur(rounded, received)

    def apply_prec(field):
        rounded = lax.optimization_barrier(field.astype(jnp.bfloat16))
        result = trace_scale * rounded.astype(jnp.float32) + jnp.dot(
            trace_mat, rounded, preferred_element_type=jnp.float32
        )
        coarse = jnp.dot(vectors, rounded, preferred_element_type=jnp.float32)
        line = gather_rows(coarse, "gy")
        partial = jnp.dot(coarse_block, line, precision=lax.Precision.HIGHEST)
        pieces = lax.all_to_all(partial, "gx", 0, 0, tiled=True)
        solved = jnp.sum(pieces.reshape(count_x, depth, pieces.shape[-1]), axis=0)
        return result + jnp.dot(vectors_wide, solved, precision=lax.Precision.HIGHEST)

    solution = jnp.zeros(rhs_wide.shape, jnp.float32)
    direction = apply_prec(rhs_wide)
    image = apply_schur(direction)
    for iteration in range(ITERS):
        mapped = apply_prec(image)
        line_total = total_over_axis(
            jnp.stack([jnp.sum(mapped * direction, axis=0), jnp.sum(mapped * mapped, axis=0)]), "gy"
        )
        after = line_total[0, 0]
        if iteration + 1 < ITERS:
            pair = send_early(direction, mapped, after)
        else:
            pair = send_early(solution, direction, after)
        numer, denom = total_over_axis(line_total, "gx")
        alpha = numer / denom
        solution = solution + alpha * direction
        direction = direction + (-alpha) * mapped
        if iteration + 1 < ITERS:
            image = apply_schur_late(direction, pair, -alpha)
    residual = rhs_wide - apply_schur_late(solution, pair, alpha)
    return (solution[None, None], residual[None, None])


def solution(mesh):
    return jax.shard_map(
        shards,
        mesh=mesh,
        in_specs=(
            P("gx", "gy", None, None),
            P("gx", "gy", None, None),
            P("gx", "gy", None),
            P("gx", "gy", None, None),
            P("gx", "gy", None),
            P("gx", "gy", None, None, None),
            P("gx", "gy", None, None),
            P("gx", "gy", None, None),
            P(("gx", "gy"), None),
            P(),
        ),
        out_specs=(P("gx", "gy", None, None), P("gx", "gy", None, None)),
        check_vma=False,
    )
```

```python
import jax
import jax.numpy as jnp
from jax import lax
from jax.sharding import PartitionSpec as P

ITERS = 3


def from_behind(value, axis, steps):
    count = lax.axis_size(axis)
    leading, last = (max(0, -steps), min(count, count - steps))
    return lax.ppermute(value, axis, [(source, source + steps) for source in range(leading, last)])


def gather_rows(value, axis):
    count = lax.axis_size(axis)
    copies = jnp.broadcast_to(value[None], (count,) + value.shape)
    return lax.all_to_all(copies.reshape((-1,) + value.shape[1:]), axis, 0, 0, tiled=True)


def total_over_mesh(value, tie):
    for axis in ("gy", "gx"):
        if axis == "gx":
            value = value + 0.0 * tie
        count = lax.axis_size(axis)
        value = jnp.sum(gather_rows(value, axis).reshape((count,) + value.shape), axis=0)
    return value


def pass_columns(rows, offset):
    return from_behind(rows, "gx", offset)


def pass_lines(rows, offset):
    return from_behind(rows, "gy", offset)


def shards(
    right_side,
    schur_offdiag,
    schur_diag,
    trace_offdiag,
    trace_diag,
    couplings,
    margin_rows,
    deflation,
    coarse_inverse,
    coarse_map,
):
    rhs_wide = right_side[0, 0].astype(jnp.float32)
    schur_mat = schur_offdiag[0, 0]
    schur_scale = schur_diag[0, 0][:, None]
    trace_mat = trace_offdiag[0, 0]
    trace_scale = trace_diag[0, 0][:, None]
    coupling_blocks = couplings[0, 0]
    rows_lists = margin_rows[0, 0]
    sides, width = coupling_blocks.shape[0], coupling_blocks.shape[-1]
    placed_couplings = (
        jnp.zeros((schur_mat.shape[0], sides * width), coupling_blocks.dtype)
        .at[rows_lists[:, :, None], (jnp.arange(sides)[:, None, None] * width + jnp.arange(width))]
        .set(coupling_blocks)
    )
    vectors = deflation[0, 0]
    vectors_wide = vectors.astype(jnp.float32).T
    count_x, count_y = lax.axis_size("gx"), lax.axis_size("gy")
    depth = vectors.shape[0]
    coarse_cols = jnp.take(coarse_inverse, coarse_map, axis=1)
    coarse_block = lax.all_to_all(
        coarse_cols.reshape(depth, count_x, count_y * depth), "gx", 1, 0, tiled=True
    ).reshape(count_x * depth, count_y * depth)

    def exchange(sent_rows):
        return jnp.stack(
            [
                pass_columns(sent_rows[1], 1),
                pass_columns(sent_rows[0], -1),
                pass_lines(sent_rows[3], 1),
                pass_lines(sent_rows[2], -1),
            ]
        )

    def finish_schur(rounded, received):
        result = schur_scale * rounded.astype(jnp.float32) + jnp.dot(
            schur_mat, rounded, preferred_element_type=jnp.float32
        )
        coupled = jnp.dot(
            placed_couplings, received.reshape(-1, received.shape[-1]), preferred_element_type=jnp.float32
        )
        return result - coupled

    def apply_schur(field):
        rounded = lax.optimization_barrier(field.astype(jnp.bfloat16))
        return finish_schur(rounded, exchange(rounded[rows_lists]))

    def send_early(base, step):
        return exchange(jnp.stack([base[rows_lists], step[rows_lists]], axis=1))

    def apply_schur_late(field, pair, coef):
        rounded = lax.optimization_barrier(field.astype(jnp.bfloat16))
        received = (pair[:, 0] + coef * pair[:, 1]).astype(jnp.bfloat16)
        return finish_schur(rounded, received)

    def apply_prec(field):
        rounded = lax.optimization_barrier(field.astype(jnp.bfloat16))
        result = trace_scale * rounded.astype(jnp.float32) + jnp.dot(
            trace_mat, rounded, preferred_element_type=jnp.float32
        )
        coarse = jnp.dot(vectors, rounded, preferred_element_type=jnp.float32)
        line = gather_rows(coarse, "gy")
        partial = jnp.dot(coarse_block, line, precision=lax.Precision.HIGHEST)
        pieces = lax.all_to_all(partial, "gx", 0, 0, tiled=True)
        solved = jnp.sum(pieces.reshape(count_x, depth, pieces.shape[-1]), axis=0)
        return result + jnp.dot(vectors_wide, solved, precision=lax.Precision.HIGHEST)

    solution = jnp.zeros(rhs_wide.shape, jnp.float32)
    direction = apply_prec(rhs_wide)
    image = apply_schur(direction)
    for iteration in range(ITERS):
        mapped = apply_prec(image)
        if iteration + 1 < ITERS:
            pair = send_early(direction, mapped)
        else:
            pair = send_early(solution, direction)
        numer, denom = total_over_mesh(
            jnp.stack([jnp.sum(mapped * direction, axis=0), jnp.sum(mapped * mapped, axis=0)]),
            jnp.sum(pair[:, 0, 0, 0]),
        )
        alpha = numer / denom
        solution = solution + alpha * direction
        direction = direction + (-alpha) * mapped
        if iteration + 1 < ITERS:
            image = apply_schur_late(direction, pair, -alpha)
    residual = rhs_wide - apply_schur_late(solution, pair, alpha)
    return (solution[None, None], residual[None, None])


def solution(mesh):
    return jax.shard_map(
        shards,
        mesh=mesh,
        in_specs=(
            P("gx", "gy", None, None),
            P("gx", "gy", None, None),
            P("gx", "gy", None),
            P("gx", "gy", None, None),
            P("gx", "gy", None),
            P("gx", "gy", None, None, None),
            P("gx", "gy", None, None),
            P("gx", "gy", None, None),
            P(("gx", "gy"), None),
            P(),
        ),
        out_specs=(P("gx", "gy", None, None), P("gx", "gy", None, None)),
        check_vma=False,
    )
```

```python
import jax
import jax.numpy as jnp
from jax import lax
from jax.sharding import PartitionSpec as P

ITERS = 3


def from_behind(value, axis, steps):
    count = lax.axis_size(axis)
    leading, last = (max(0, -steps), min(count, count - steps))
    return lax.ppermute(value, axis, [(source, source + steps) for source in range(leading, last)])


def gather_rows(value, axis):
    count = lax.axis_size(axis)
    copies = jnp.broadcast_to(value[None], (count,) + value.shape)
    return lax.all_to_all(copies.reshape((-1,) + value.shape[1:]), axis, 0, 0, tiled=True)


def total_over_mesh(value, tie):
    for axis in ("gy", "gx"):
        if axis == "gx":
            value = value + 0.0 * tie
        count = lax.axis_size(axis)
        value = jnp.sum(gather_rows(value, axis).reshape((count,) + value.shape), axis=0)
    return value


def pass_columns(rows, offset):
    return from_behind(rows, "gx", offset)


def pass_lines(rows, offset):
    return from_behind(rows, "gy", offset)


def shards(
    right_side,
    schur_offdiag,
    schur_diag,
    trace_offdiag,
    trace_diag,
    couplings,
    margin_rows,
    deflation,
    coarse_inverse,
    coarse_map,
):
    rhs_wide = right_side[0, 0].astype(jnp.float32)
    schur_mat = schur_offdiag[0, 0]
    schur_scale = schur_diag[0, 0][:, None]
    trace_mat = trace_offdiag[0, 0]
    trace_scale = trace_diag[0, 0][:, None]
    coupling_blocks = couplings[0, 0]
    rows_lists = margin_rows[0, 0]
    sides, width = coupling_blocks.shape[0], coupling_blocks.shape[-1]
    selectors = (
        rows_lists[:, None, :] == jnp.arange(schur_mat.shape[0], dtype=rows_lists.dtype)[None, :, None]
    ).astype(coupling_blocks.dtype)
    placed_couplings = (
        jnp.einsum("dra,dab->rdb", selectors, coupling_blocks, preferred_element_type=jnp.float32)
        .astype(coupling_blocks.dtype)
        .reshape(schur_mat.shape[0], sides * width)
    )
    vectors = deflation[0, 0]
    vectors_wide = vectors.astype(jnp.float32).T
    count_x, count_y = lax.axis_size("gx"), lax.axis_size("gy")
    depth = vectors.shape[0]
    coarse_cols = jnp.take(coarse_inverse, coarse_map, axis=1)
    coarse_block = lax.all_to_all(
        coarse_cols.reshape(depth, count_x, count_y * depth), "gx", 1, 0, tiled=True
    ).reshape(count_x * depth, count_y * depth)

    def exchange(sent_rows):
        return jnp.stack(
            [
                pass_columns(sent_rows[1], 1),
                pass_columns(sent_rows[0], -1),
                pass_lines(sent_rows[3], 1),
                pass_lines(sent_rows[2], -1),
            ]
        )

    def finish_schur(rounded, received):
        result = schur_scale * rounded.astype(jnp.float32) + jnp.dot(
            schur_mat, rounded, preferred_element_type=jnp.float32
        )
        coupled = jnp.dot(
            placed_couplings, received.reshape(-1, received.shape[-1]), preferred_element_type=jnp.float32
        )
        return result - coupled

    def apply_schur(field):
        rounded = lax.optimization_barrier(field.astype(jnp.bfloat16))
        return finish_schur(rounded, exchange(rounded[rows_lists]))

    def send_early(base, step):
        return exchange(jnp.stack([base[rows_lists], step[rows_lists]], axis=1))

    def apply_schur_late(field, pair, coef):
        rounded = lax.optimization_barrier(field.astype(jnp.bfloat16))
        received = (pair[:, 0] + coef * pair[:, 1]).astype(jnp.bfloat16)
        return finish_schur(rounded, received)

    def apply_prec(field):
        rounded = lax.optimization_barrier(field.astype(jnp.bfloat16))
        result = trace_scale * rounded.astype(jnp.float32) + jnp.dot(
            trace_mat, rounded, preferred_element_type=jnp.float32
        )
        coarse = jnp.dot(vectors, rounded, preferred_element_type=jnp.float32)
        line = gather_rows(coarse, "gy")
        partial = jnp.dot(coarse_block, line, precision=lax.Precision.HIGHEST)
        pieces = lax.all_to_all(partial, "gx", 0, 0, tiled=True)
        solved = jnp.sum(pieces.reshape(count_x, depth, pieces.shape[-1]), axis=0)
        return result + jnp.dot(vectors_wide, solved, precision=lax.Precision.HIGHEST)

    solution = jnp.zeros(rhs_wide.shape, jnp.float32)
    direction = apply_prec(rhs_wide)
    image = apply_schur(direction)
    for iteration in range(ITERS):
        mapped = apply_prec(image)
        if iteration + 1 < ITERS:
            pair = send_early(direction, mapped)
        else:
            pair = send_early(solution, direction)
        numer, denom = total_over_mesh(
            jnp.stack([jnp.sum(mapped * direction, axis=0), jnp.sum(mapped * mapped, axis=0)]),
            jnp.sum(pair[:, 0, 0, 0]),
        )
        alpha = numer / denom
        solution = solution + alpha * direction
        direction = direction + (-alpha) * mapped
        if iteration + 1 < ITERS:
            image = apply_schur_late(direction, pair, -alpha)
    residual = rhs_wide - apply_schur_late(solution, pair, alpha)
    return (solution[None, None], residual[None, None])


def solution(mesh):
    return jax.shard_map(
        shards,
        mesh=mesh,
        in_specs=(
            P("gx", "gy", None, None),
            P("gx", "gy", None, None),
            P("gx", "gy", None),
            P("gx", "gy", None, None),
            P("gx", "gy", None),
            P("gx", "gy", None, None, None),
            P("gx", "gy", None, None),
            P("gx", "gy", None, None),
            P(("gx", "gy"), None),
            P(),
        ),
        out_specs=(P("gx", "gy", None, None), P("gx", "gy", None, None)),
        check_vma=False,
    )
```

```python
import jax
import jax.numpy as jnp
from jax import lax
from jax.sharding import PartitionSpec as P

ITERS = 3


def from_behind(value, axis, steps):
    count = lax.axis_size(axis)
    leading, last = (max(0, -steps), min(count, count - steps))
    return lax.ppermute(value, axis, [(source, source + steps) for source in range(leading, last)])


def gather_rows(value, axis):
    count = lax.axis_size(axis)
    copies = jnp.broadcast_to(value[None], (count,) + value.shape)
    return lax.all_to_all(copies.reshape((-1,) + value.shape[1:]), axis, 0, 0, tiled=True)


def total_over_mesh(value, tie):
    for axis in ("gy", "gx"):
        if axis == "gx":
            value = value + 0.0 * tie
        count = lax.axis_size(axis)
        value = jnp.sum(gather_rows(value, axis).reshape((count,) + value.shape), axis=0)
    return value


def pass_columns(rows, offset):
    return from_behind(rows, "gx", offset)


def pass_lines(rows, offset):
    return from_behind(rows, "gy", offset)


def shards(
    right_side,
    schur_offdiag,
    schur_diag,
    trace_offdiag,
    trace_diag,
    couplings,
    margin_rows,
    deflation,
    coarse_inverse,
    coarse_map,
):
    rhs_wide = right_side[0, 0].astype(jnp.float32)
    schur_mat = schur_offdiag[0, 0]
    schur_scale = schur_diag[0, 0][:, None]
    trace_mat = trace_offdiag[0, 0]
    trace_scale = trace_diag[0, 0][:, None]
    coupling_blocks = couplings[0, 0]
    rows_lists = margin_rows[0, 0]
    sides, width = coupling_blocks.shape[0], coupling_blocks.shape[-1]
    selectors = (
        rows_lists[:, None, :] == jnp.arange(schur_mat.shape[0], dtype=rows_lists.dtype)[None, :, None]
    ).astype(coupling_blocks.dtype)
    placed_couplings = (
        jnp.einsum("dra,dab->rdb", selectors, coupling_blocks, preferred_element_type=jnp.float32)
        .astype(coupling_blocks.dtype)
        .reshape(schur_mat.shape[0], sides * width)
    )
    schur_with_couplings = jnp.concatenate([schur_mat, -placed_couplings], axis=1)
    vectors = deflation[0, 0]
    vectors_wide = vectors.astype(jnp.float32).T
    count_x, count_y = lax.axis_size("gx"), lax.axis_size("gy")
    depth = vectors.shape[0]
    coarse_cols = jnp.take(coarse_inverse, coarse_map, axis=1)
    coarse_block = lax.all_to_all(
        coarse_cols.reshape(depth, count_x, count_y * depth), "gx", 1, 0, tiled=True
    ).reshape(count_x * depth, count_y * depth)

    def exchange(sent_rows):
        return jnp.stack(
            [
                pass_columns(sent_rows[1], 1),
                pass_columns(sent_rows[0], -1),
                pass_lines(sent_rows[3], 1),
                pass_lines(sent_rows[2], -1),
            ]
        )

    def finish_schur(rounded, received):
        stacked = jnp.concatenate([rounded, received.reshape(-1, received.shape[-1])], axis=0)
        return schur_scale * rounded.astype(jnp.float32) + jnp.dot(
            schur_with_couplings, stacked, preferred_element_type=jnp.float32
        )

    def apply_schur(field):
        rounded = lax.optimization_barrier(field.astype(jnp.bfloat16))
        return finish_schur(rounded, exchange(rounded[rows_lists]))

    def send_early(base, step):
        return exchange(jnp.stack([base[rows_lists], step[rows_lists]], axis=1))

    def apply_schur_late(field, pair, coef):
        rounded = lax.optimization_barrier(field.astype(jnp.bfloat16))
        received = (pair[:, 0] + coef * pair[:, 1]).astype(jnp.bfloat16)
        return finish_schur(rounded, received)

    def apply_prec(field):
        rounded = lax.optimization_barrier(field.astype(jnp.bfloat16))
        result = trace_scale * rounded.astype(jnp.float32) + jnp.dot(
            trace_mat, rounded, preferred_element_type=jnp.float32
        )
        coarse = jnp.dot(vectors, rounded, preferred_element_type=jnp.float32)
        line = gather_rows(coarse, "gy")
        partial = jnp.dot(coarse_block, line, precision=lax.Precision.HIGHEST)
        pieces = lax.all_to_all(partial, "gx", 0, 0, tiled=True)
        solved = jnp.sum(pieces.reshape(count_x, depth, pieces.shape[-1]), axis=0)
        return result + jnp.dot(vectors_wide, solved, precision=lax.Precision.HIGHEST)

    solution = jnp.zeros(rhs_wide.shape, jnp.float32)
    direction = apply_prec(rhs_wide)
    image = apply_schur(direction)
    for iteration in range(ITERS):
        mapped = apply_prec(image)
        if iteration + 1 < ITERS:
            pair = send_early(direction, mapped)
        else:
            pair = send_early(solution, direction)
        numer, denom = total_over_mesh(
            jnp.stack([jnp.sum(mapped * direction, axis=0), jnp.sum(mapped * mapped, axis=0)]),
            jnp.sum(pair[:, 0, 0, 0]),
        )
        alpha = numer / denom
        solution = solution + alpha * direction
        direction = direction + (-alpha) * mapped
        if iteration + 1 < ITERS:
            image = apply_schur_late(direction, pair, -alpha)
    residual = rhs_wide - apply_schur_late(solution, pair, alpha)
    return (solution[None, None], residual[None, None])


def solution(mesh):
    return jax.shard_map(
        shards,
        mesh=mesh,
        in_specs=(
            P("gx", "gy", None, None),
            P("gx", "gy", None, None),
            P("gx", "gy", None),
            P("gx", "gy", None, None),
            P("gx", "gy", None),
            P("gx", "gy", None, None, None),
            P("gx", "gy", None, None),
            P("gx", "gy", None, None),
            P(("gx", "gy"), None),
            P(),
        ),
        out_specs=(P("gx", "gy", None, None), P("gx", "gy", None, None)),
        check_vma=False,
    )
```

```python
import jax
import jax.numpy as jnp
from jax import lax
from jax.sharding import PartitionSpec as P

ITERS = 3


def from_behind(value, axis, steps):
    count = lax.axis_size(axis)
    leading, last = (max(0, -steps), min(count, count - steps))
    return lax.ppermute(value, axis, [(source, source + steps) for source in range(leading, last)])


def gather_rows(value, axis):
    count = lax.axis_size(axis)
    copies = jnp.broadcast_to(value[None], (count,) + value.shape)
    return lax.all_to_all(copies.reshape((-1,) + value.shape[1:]), axis, 0, 0, tiled=True)


def total_over_mesh(value, tie):
    for axis in ("gy", "gx"):
        if axis == "gx":
            value = value + 0.0 * tie
        count = lax.axis_size(axis)
        value = jnp.sum(gather_rows(value, axis).reshape((count,) + value.shape), axis=0)
    return value


def pass_columns(rows, offset):
    return from_behind(rows, "gx", offset)


def pass_lines(rows, offset):
    return from_behind(rows, "gy", offset)


def shards(
    right_side,
    schur_offdiag,
    schur_diag,
    trace_offdiag,
    trace_diag,
    couplings,
    margin_rows,
    deflation,
    coarse_inverse,
    coarse_map,
):
    rhs_wide = right_side[0, 0].astype(jnp.float32)
    schur_mat = schur_offdiag[0, 0]
    schur_scale = schur_diag[0, 0][:, None]
    trace_mat = trace_offdiag[0, 0]
    trace_scale = trace_diag[0, 0][:, None]
    coupling_blocks = couplings[0, 0]
    rows_lists = margin_rows[0, 0]
    sides, width = coupling_blocks.shape[0], coupling_blocks.shape[-1]
    selectors = (
        rows_lists[:, None, :] == jnp.arange(schur_mat.shape[0], dtype=rows_lists.dtype)[None, :, None]
    ).astype(coupling_blocks.dtype)
    placed_couplings = (
        jnp.einsum("dra,dab->rdb", selectors, coupling_blocks, preferred_element_type=jnp.float32)
        .astype(coupling_blocks.dtype)
        .reshape(schur_mat.shape[0], sides * width)
    )
    schur_with_couplings = jnp.concatenate([schur_mat, -placed_couplings], axis=1)
    vectors = deflation[0, 0]
    vectors_wide = vectors.astype(jnp.float32).T
    trace_with_vectors = jnp.concatenate([vectors, trace_mat], axis=0)
    count_x, count_y = lax.axis_size("gx"), lax.axis_size("gy")
    depth = vectors.shape[0]
    coarse_cols = jnp.take(coarse_inverse, coarse_map, axis=1)
    coarse_block = lax.all_to_all(
        coarse_cols.reshape(depth, count_x, count_y * depth), "gx", 1, 0, tiled=True
    ).reshape(count_x * depth, count_y * depth)

    def exchange(sent_rows):
        return jnp.stack(
            [
                pass_columns(sent_rows[1], 1),
                pass_columns(sent_rows[0], -1),
                pass_lines(sent_rows[3], 1),
                pass_lines(sent_rows[2], -1),
            ]
        )

    def finish_schur(rounded, received):
        stacked = jnp.concatenate([rounded, received.reshape(-1, received.shape[-1])], axis=0)
        return schur_scale * rounded.astype(jnp.float32) + jnp.dot(
            schur_with_couplings, stacked, preferred_element_type=jnp.float32
        )

    def apply_schur(field):
        rounded = lax.optimization_barrier(field.astype(jnp.bfloat16))
        return finish_schur(rounded, exchange(rounded[rows_lists]))

    def send_early(base, step):
        return exchange(jnp.stack([base[rows_lists], step[rows_lists]], axis=1))

    def apply_schur_late(field, pair, coef):
        rounded = lax.optimization_barrier(field.astype(jnp.bfloat16))
        received = (pair[:, 0] + coef * pair[:, 1]).astype(jnp.bfloat16)
        return finish_schur(rounded, received)

    def apply_prec(field):
        rounded = lax.optimization_barrier(field.astype(jnp.bfloat16))
        both = jnp.dot(trace_with_vectors, rounded, preferred_element_type=jnp.float32)
        coarse = both[: vectors.shape[0]]
        result = trace_scale * rounded.astype(jnp.float32) + both[vectors.shape[0] :]
        line = gather_rows(coarse, "gy")
        partial = jnp.dot(coarse_block, line, precision=lax.Precision.HIGHEST)
        pieces = lax.all_to_all(partial, "gx", 0, 0, tiled=True)
        solved = jnp.sum(pieces.reshape(count_x, depth, pieces.shape[-1]), axis=0)
        return result + jnp.dot(vectors_wide, solved, precision=lax.Precision.HIGHEST)

    solution = jnp.zeros(rhs_wide.shape, jnp.float32)
    direction = apply_prec(rhs_wide)
    image = apply_schur(direction)
    for iteration in range(ITERS):
        mapped = apply_prec(image)
        if iteration + 1 < ITERS:
            pair = send_early(direction, mapped)
        else:
            pair = send_early(solution, direction)
        numer, denom = total_over_mesh(
            jnp.stack([jnp.sum(mapped * direction, axis=0), jnp.sum(mapped * mapped, axis=0)]),
            jnp.sum(pair[:, 0, 0, 0]),
        )
        alpha = numer / denom
        solution = solution + alpha * direction
        direction = direction + (-alpha) * mapped
        if iteration + 1 < ITERS:
            image = apply_schur_late(direction, pair, -alpha)
    residual = rhs_wide - apply_schur_late(solution, pair, alpha)
    return (solution[None, None], residual[None, None])


def solution(mesh):
    return jax.shard_map(
        shards,
        mesh=mesh,
        in_specs=(
            P("gx", "gy", None, None),
            P("gx", "gy", None, None),
            P("gx", "gy", None),
            P("gx", "gy", None, None),
            P("gx", "gy", None),
            P("gx", "gy", None, None, None),
            P("gx", "gy", None, None),
            P("gx", "gy", None, None),
            P(("gx", "gy"), None),
            P(),
        ),
        out_specs=(P("gx", "gy", None, None), P("gx", "gy", None, None)),
        check_vma=False,
    )
```

```python
import jax
import jax.numpy as jnp
from jax import lax
from jax.sharding import PartitionSpec as P

ITERS = 3


def from_behind(value, axis, steps):
    count = lax.axis_size(axis)
    leading, last = (max(0, -steps), min(count, count - steps))
    return lax.ppermute(value, axis, [(source, source + steps) for source in range(leading, last)])


def gather_rows(value, axis):
    count = lax.axis_size(axis)
    copies = jnp.broadcast_to(value[None], (count,) + value.shape)
    return lax.all_to_all(copies.reshape((-1,) + value.shape[1:]), axis, 0, 0, tiled=True)


def total_over_mesh(value, tie):
    for axis in ("gy", "gx"):
        if axis == "gx":
            value = value + 0.0 * tie
        count = lax.axis_size(axis)
        value = jnp.sum(gather_rows(value, axis).reshape((count,) + value.shape), axis=0)
    return value


def pass_columns(rows, offset):
    return from_behind(rows, "gx", offset)


def pass_lines(rows, offset):
    return from_behind(rows, "gy", offset)


def shards(
    right_side,
    schur_offdiag,
    schur_diag,
    trace_offdiag,
    trace_diag,
    couplings,
    margin_rows,
    deflation,
    coarse_inverse,
    coarse_map,
):
    rhs_wide = right_side[0, 0].astype(jnp.float32)
    schur_mat = schur_offdiag[0, 0]
    schur_scale = schur_diag[0, 0][:, None]
    trace_mat = trace_offdiag[0, 0]
    trace_scale = trace_diag[0, 0][:, None]
    coupling_blocks = couplings[0, 0]
    rows_lists = margin_rows[0, 0]
    sides, width = coupling_blocks.shape[0], coupling_blocks.shape[-1]
    selectors = (
        rows_lists[:, None, :] == jnp.arange(schur_mat.shape[0], dtype=rows_lists.dtype)[None, :, None]
    ).astype(coupling_blocks.dtype)
    placed_couplings = (
        jnp.einsum("dra,dab->rdb", selectors, coupling_blocks, preferred_element_type=jnp.float32)
        .astype(coupling_blocks.dtype)
        .reshape(schur_mat.shape[0], sides * width)
    )
    schur_with_couplings = jnp.concatenate([schur_mat, -placed_couplings], axis=1)
    vectors = deflation[0, 0]
    vectors_wide = vectors.astype(jnp.float32).T
    trace_with_vectors = jnp.concatenate([vectors, trace_mat], axis=0)
    count_x, count_y = lax.axis_size("gx"), lax.axis_size("gy")
    depth = vectors.shape[0]
    coarse_cols = jnp.take(coarse_inverse, coarse_map, axis=1)
    coarse_block = lax.all_to_all(
        coarse_cols.reshape(depth, count_x, count_y * depth), "gx", 1, 0, tiled=True
    ).reshape(count_x * depth, count_y * depth)

    def exchange(sent_rows):
        return jnp.stack(
            [
                pass_columns(sent_rows[1], 1),
                pass_columns(sent_rows[0], -1),
                pass_lines(sent_rows[3], 1),
                pass_lines(sent_rows[2], -1),
            ]
        )

    def finish_schur(rounded, received):
        stacked = jnp.concatenate([rounded, received.reshape(-1, received.shape[-1])], axis=0)
        return schur_scale * rounded.astype(jnp.float32) + jnp.dot(
            schur_with_couplings, stacked, preferred_element_type=jnp.float32
        )

    def apply_schur(field):
        rounded = lax.optimization_barrier(field.astype(jnp.bfloat16))
        return finish_schur(rounded, exchange(rounded[rows_lists]))

    def send_early(base, step):
        return exchange(jnp.stack([base[rows_lists], step[rows_lists]], axis=1))

    def apply_schur_late(field, pair, coef):
        rounded = lax.optimization_barrier(field.astype(jnp.bfloat16))
        received = (pair[:, 0] + coef * pair[:, 1]).astype(jnp.bfloat16)
        return finish_schur(rounded, received)

    def apply_prec(field):
        rounded = lax.optimization_barrier(field.astype(jnp.bfloat16))
        both = jnp.dot(trace_with_vectors, rounded, preferred_element_type=jnp.float32)
        coarse = both[: vectors.shape[0]]
        result = trace_scale * rounded.astype(jnp.float32) + both[vectors.shape[0] :]
        line = gather_rows(coarse, "gy")
        partial = jnp.dot(coarse_block, line, precision=lax.Precision.HIGH)
        pieces = lax.all_to_all(partial, "gx", 0, 0, tiled=True)
        solved = jnp.sum(pieces.reshape(count_x, depth, pieces.shape[-1]), axis=0)
        return result + jnp.dot(vectors_wide, solved, precision=lax.Precision.HIGH)

    solution = jnp.zeros(rhs_wide.shape, jnp.float32)
    direction = apply_prec(rhs_wide)
    image = apply_schur(direction)
    for iteration in range(ITERS):
        mapped = apply_prec(image)
        if iteration + 1 < ITERS:
            pair = send_early(direction, mapped)
        else:
            pair = send_early(solution, direction)
        numer, denom = total_over_mesh(
            jnp.stack([jnp.sum(mapped * direction, axis=0), jnp.sum(mapped * mapped, axis=0)]),
            jnp.sum(pair[:, 0, 0, 0]),
        )
        alpha = numer / denom
        solution = solution + alpha * direction
        direction = direction + (-alpha) * mapped
        if iteration + 1 < ITERS:
            image = apply_schur_late(direction, pair, -alpha)
    residual = rhs_wide - apply_schur_late(solution, pair, alpha)
    return (solution[None, None], residual[None, None])


def solution(mesh):
    return jax.shard_map(
        shards,
        mesh=mesh,
        in_specs=(
            P("gx", "gy", None, None),
            P("gx", "gy", None, None),
            P("gx", "gy", None),
            P("gx", "gy", None, None),
            P("gx", "gy", None),
            P("gx", "gy", None, None, None),
            P("gx", "gy", None, None),
            P("gx", "gy", None, None),
            P(("gx", "gy"), None),
            P(),
        ),
        out_specs=(P("gx", "gy", None, None), P("gx", "gy", None, None)),
        check_vma=False,
    )
```

```python
import jax
import jax.numpy as jnp
from jax import lax
from jax.sharding import PartitionSpec as P

ITERS = 3


def from_behind(value, axis, steps):
    count = lax.axis_size(axis)
    leading, last = (max(0, -steps), min(count, count - steps))
    return lax.ppermute(value, axis, [(source, source + steps) for source in range(leading, last)])


def gather_rows(value, axis):
    count = lax.axis_size(axis)
    copies = jnp.broadcast_to(value[None], (count,) + value.shape)
    return lax.all_to_all(copies.reshape((-1,) + value.shape[1:]), axis, 0, 0, tiled=True)


def total_over_mesh(value, tie):
    for axis in ("gx", "gy"):
        if axis == "gy":
            value = value + 0.0 * tie
        count = lax.axis_size(axis)
        value = jnp.sum(gather_rows(value, axis).reshape((count,) + value.shape), axis=0)
    return value


def pass_columns(rows, offset):
    return from_behind(rows, "gx", offset)


def pass_lines(rows, offset):
    return from_behind(rows, "gy", offset)


def shards(
    right_side,
    schur_offdiag,
    schur_diag,
    trace_offdiag,
    trace_diag,
    couplings,
    margin_rows,
    deflation,
    coarse_inverse,
    coarse_map,
):
    rhs_wide = right_side[0, 0].astype(jnp.float32)
    schur_mat = schur_offdiag[0, 0]
    schur_scale = schur_diag[0, 0][:, None]
    trace_mat = trace_offdiag[0, 0]
    trace_scale = trace_diag[0, 0][:, None]
    coupling_blocks = couplings[0, 0]
    rows_lists = margin_rows[0, 0]
    sides, width = coupling_blocks.shape[0], coupling_blocks.shape[-1]
    selectors = (
        rows_lists[:, None, :] == jnp.arange(schur_mat.shape[0], dtype=rows_lists.dtype)[None, :, None]
    ).astype(coupling_blocks.dtype)
    placed_couplings = (
        jnp.einsum("dra,dab->rdb", selectors, coupling_blocks, preferred_element_type=jnp.float32)
        .astype(coupling_blocks.dtype)
        .reshape(schur_mat.shape[0], sides * width)
    )
    schur_with_couplings = jnp.concatenate([schur_mat, -placed_couplings], axis=1)
    vectors = deflation[0, 0]
    vectors_wide = vectors.astype(jnp.float32).T
    trace_with_vectors = jnp.concatenate([vectors, trace_mat], axis=0)
    count_x, count_y = lax.axis_size("gx"), lax.axis_size("gy")
    depth = vectors.shape[0]
    coarse_cols = jnp.take(coarse_inverse, coarse_map, axis=1)
    coarse_block = lax.all_to_all(
        coarse_cols.reshape(depth, count_x, count_y * depth), "gx", 1, 0, tiled=True
    ).reshape(count_x * depth, count_y * depth)

    def exchange(sent_rows):
        return jnp.stack(
            [
                pass_columns(sent_rows[1], 1),
                pass_columns(sent_rows[0], -1),
                pass_lines(sent_rows[3], 1),
                pass_lines(sent_rows[2], -1),
            ]
        )

    def finish_schur(rounded, received):
        stacked = jnp.concatenate([rounded, received.reshape(-1, received.shape[-1])], axis=0)
        return schur_scale * rounded.astype(jnp.float32) + jnp.dot(
            schur_with_couplings, stacked, preferred_element_type=jnp.float32
        )

    def apply_schur(field):
        rounded = lax.optimization_barrier(field.astype(jnp.bfloat16))
        return finish_schur(rounded, exchange(rounded[rows_lists]))

    def send_early(base, step):
        return exchange(jnp.stack([base[rows_lists], step[rows_lists]], axis=1))

    def apply_schur_late(field, pair, coef):
        rounded = lax.optimization_barrier(field.astype(jnp.bfloat16))
        received = (pair[:, 0] + coef * pair[:, 1]).astype(jnp.bfloat16)
        return finish_schur(rounded, received)

    def apply_prec(field):
        rounded = lax.optimization_barrier(field.astype(jnp.bfloat16))
        both = jnp.dot(trace_with_vectors, rounded, preferred_element_type=jnp.float32)
        coarse = both[: vectors.shape[0]]
        result = trace_scale * rounded.astype(jnp.float32) + both[vectors.shape[0] :]
        line = gather_rows(coarse, "gy")
        partial = jnp.dot(coarse_block, line, precision=lax.Precision.HIGHEST)
        pieces = lax.all_to_all(partial, "gx", 0, 0, tiled=True)
        solved = jnp.sum(pieces.reshape(count_x, depth, pieces.shape[-1]), axis=0)
        return result + jnp.dot(vectors_wide, solved, precision=lax.Precision.HIGHEST)

    solution = jnp.zeros(rhs_wide.shape, jnp.float32)
    direction = apply_prec(rhs_wide)
    image = apply_schur(direction)
    for iteration in range(ITERS):
        mapped = apply_prec(image)
        if iteration + 1 < ITERS:
            pair = send_early(direction, mapped)
        else:
            pair = send_early(solution, direction)
        numer, denom = total_over_mesh(
            jnp.stack([jnp.sum(mapped * direction, axis=0), jnp.sum(mapped * mapped, axis=0)]),
            jnp.sum(pair[:, 0, 0, 0]),
        )
        alpha = numer / denom
        solution = solution + alpha * direction
        direction = direction + (-alpha) * mapped
        if iteration + 1 < ITERS:
            image = apply_schur_late(direction, pair, -alpha)
    residual = rhs_wide - apply_schur_late(solution, pair, alpha)
    return (solution[None, None], residual[None, None])


def solution(mesh):
    return jax.shard_map(
        shards,
        mesh=mesh,
        in_specs=(
            P("gx", "gy", None, None),
            P("gx", "gy", None, None),
            P("gx", "gy", None),
            P("gx", "gy", None, None),
            P("gx", "gy", None),
            P("gx", "gy", None, None, None),
            P("gx", "gy", None, None),
            P("gx", "gy", None, None),
            P(("gx", "gy"), None),
            P(),
        ),
        out_specs=(P("gx", "gy", None, None), P("gx", "gy", None, None)),
        check_vma=False,
    )
```
